128 devices in a mesh: dp: 16 (over y, x_lo, core), feat: 8 (over x_hi, z).
Axes of the slice: x: 4 (x_hi: 2, x_lo: 2; x = x_hi * 2 + x_lo), y: 4, z: 4, core: 2. Of those that a mesh axis runs over, the one named last changes fastest.
Arguments:
- dataset: bfloat16 [131072, 4096], P('dp', 'feat'), may hold values from -0.09375 to 0.09375
- targets: float32 [131072], P('dp'), may hold values from 0 to 1
- indices: int32 [32768], P('dp'), may hold values from 0 to 8191
- particles: bfloat16 [1536, 4096], P('dp', 'feat'), may hold values from -6 to 6
- spread: int32 [1], replicated, may hold values from 2048 to 8191
Outputs:
- attraction: float32 [1536, 4096], P('dp', 'feat')
- repulsion: float32 [1536, 4096], P('dp', 'feat')
The draws below stay inside these ranges and needn't reach their ends.
Inputs may be any that keep to these rules, and one draw needn't show every extreme that they name: Entry r of indices names a row within block r // 2048 of the dataset's blocks of 8192 rows.
All inputs are finite; a program needn't handle non-finite values.
Results may differ from the reference program's by a relative error of at most 0.00115.
Values may be sent and summed in bfloat16 or wider, within the bound.
No kernel may reach another device: no remote copies, remote signals or barrier semaphores. Data moves between devices by JAX's collectives and lax.ppermute only.
A program may use at most 128 MiB of HBM per device.

```python
import jax
import jax.numpy as jnp
from jax import lax

D = 4096
B_DEV = 2048
DS_DEV = 8192
PARTICLES = 1536
BATCH = 32768
DATA = 131072
N_FEAT = 8


def with_ends(values, stream_key, low, high):
    longest = values.shape.index(max(values.shape))
    spots = []
    for shift in (0, 1):
        where = [jax.random.randint(jax.random.fold_in(stream_key, axis), (), 0, length) for axis, length in enumerate(values.shape)]
        where[longest] = (where[longest] + shift) % values.shape[longest]
        spots.append(tuple(where))
    return values.at[spots[0]].set(low).at[spots[1]].set(high)


def block_scale(rng, extent, pieces, smallest, top_value):
    gain, own = 1.0, jax.random.fold_in(rng, 6)
    for dim, parts in pieces:
        steps = jnp.exp(jax.random.uniform(jax.random.fold_in(own, dim), (parts,), jnp.float32, smallest / len(pieces), top_value / len(pieces)))
        gain = gain * jnp.repeat(steps, extent[dim] // parts).reshape([-1 if axis == dim else 1 for axis in range(len(extent))])
    return gain


def noise(own_key, shape, scale, limit, shards=(), kind=jnp.bfloat16):
    array = jax.random.normal(own_key, shape, jnp.float32) * scale
    if len(shards) > 0:
        array = block_scale(own_key, shape, shards, -0.22, 0.18) * array
    return jnp.clip(array, min=-limit, max=limit).astype(kind)


def setup_inputs(seed: int = 0) -> dict:
    key_of = jax.random.split(jax.random.key(seed), 6)
    dataset = noise(key_of[0], (DATA, D), D ** -0.5, 0.09375, ((0, 16), (1, 8)))
    targets = jnp.clip(1.0 * jax.random.uniform(key_of[1], (DATA,), jnp.float32) ** block_scale(key_of[1], (DATA,), ((0, 16),), -0.2, 0.2), 0.0, 1.0)
    indices = with_ends(jax.random.randint(key_of[2], (BATCH,), 0, DS_DEV), jax.random.fold_in(key_of[2], 1), 0, DS_DEV - 1).astype(jnp.int32)
    particles = noise(key_of[3], (PARTICLES, D), 1.0, 6.0, ((0, 16), (1, 8)))
    spread = jax.random.randint(key_of[4], (1,), D // 2, 2 * D).astype(jnp.int32)
    return {"dataset": dataset, "targets": targets, "indices": indices, "particles": particles, "spread": spread}


def reference(dataset, targets, indices, particles, spread):
    row_ids = jnp.arange(BATCH, dtype=jnp.int32)
    rows = (row_ids // B_DEV) * DS_DEV + indices.astype(jnp.int32)
    batch_x = dataset[rows]
    batch_t = targets[rows]
    feat_width = D // N_FEAT
    logits = jnp.zeros((BATCH, PARTICLES), jnp.float32)
    for column in range(N_FEAT):
        low = column * feat_width
        piece_sum = jnp.dot(batch_x[:, low:low + feat_width], particles[:, low:low + feat_width].T, preferred_element_type=jnp.float32)
        rounded = lax.optimization_barrier(piece_sum.astype(jnp.bfloat16))
        logits = logits + rounded.astype(jnp.float32)
    residual = (batch_t[:, None] - jax.nn.sigmoid(logits)).astype(jnp.bfloat16)
    gradient = jnp.dot(residual.T, batch_x, preferred_element_type=jnp.float32)
    theta_f = particles.astype(jnp.float32)
    score = (DS_DEV / B_DEV) * gradient - theta_f
    sq_norms = jnp.sum(theta_f * theta_f, axis=1)
    inner = jnp.dot(particles, particles.T, preferred_element_type=jnp.float32)
    scale_h = spread[0].astype(jnp.float32)
    kernel = jnp.exp(-(sq_norms[:, None] + sq_norms[None, :] - 2.0 * inner) / scale_h)
    attraction = jnp.dot(kernel, score, precision=lax.Precision.HIGHEST) / PARTICLES
    pulled = jnp.dot(kernel, theta_f, precision=lax.Precision.HIGHEST)
    repulsion = (theta_f * jnp.sum(kernel, axis=1)[:, None] - pulled) / PARTICLES
    return attraction, repulsion
```

```python
import jax
import jax.numpy as jnp
from jax import lax
from jax.sharding import PartitionSpec as P


def contract(left, right):
    return lax.dot_general(
        left, right, (((1,), (1,)), ((), ())), preferred_element_type=jnp.float32
    )


def exact_dot(left, right):
    return jnp.dot(left, right, precision=lax.Precision.HIGHEST)


def body(dataset, targets, indices, particles, spread):
    batch_x = jnp.take(dataset, indices, axis=0)
    batch_t = jnp.take(targets, indices, axis=0)
    data_ratio = dataset.shape[0] / indices.shape[0]
    scale_h = spread[0].astype(jnp.float32)
    all_rows = lax.all_gather(particles, "dp", axis=0, tiled=True)
    count_all = all_rows.shape[0]
    rows_own = particles.shape[0]
    inner_part = contract(particles, all_rows)
    theta_all = all_rows.astype(jnp.float32)
    sq_part = jnp.sum(theta_all * theta_all, axis=1)
    packed = lax.psum(jnp.concatenate([inner_part, sq_part[None, :]], axis=0), "feat")
    inner = packed[:rows_own]
    norms_b = packed[rows_own]
    own_sq = lax.dynamic_slice_in_dim(norms_b, lax.axis_index("dp") * rows_own, rows_own, 0)
    partial_value = contract(batch_x, all_rows)
    own_logits = lax.psum_scatter(
        partial_value.astype(jnp.bfloat16), "feat", scatter_dimension=1, tiled=True
    ).astype(jnp.float32)
    own_residual = (batch_t[:, None] - jax.nn.sigmoid(own_logits)).astype(jnp.bfloat16)
    residual = lax.all_gather(own_residual, "feat", axis=1, tiled=True)
    gradient = lax.psum(
        lax.dot_general(
            residual, batch_x, (((0,), (0,)), ((), ())), preferred_element_type=jnp.float32
        ),
        "dp",
    )
    score = data_ratio * gradient - theta_all
    kernel = jnp.exp(-(own_sq[:, None] + norms_b[None, :] - 2.0 * inner) / scale_h)
    pushed = exact_dot(kernel, score)
    pulled = exact_dot(kernel, theta_all)
    weight = jnp.sum(kernel, axis=1)
    attraction = pushed / count_all
    repulsion = (particles.astype(jnp.float32) * weight[:, None] - pulled) / count_all
    return attraction, repulsion


def solution(mesh):
    return jax.shard_map(
        body,
        mesh=mesh,
        in_specs=(P("dp", "feat"), P("dp"), P("dp"), P("dp", "feat"), P()),
        out_specs=(P("dp", "feat"), P("dp", "feat")),
        check_vma=False,
    )
```

```python
import jax
import jax.numpy as jnp
from jax import lax
from jax.sharding import PartitionSpec as P


def contract(left, right):
    return lax.dot_general(
        left, right, (((1,), (1,)), ((), ())), preferred_element_type=jnp.float32
    )


def exact_dot(left, right):
    return jnp.dot(left, right, precision=lax.Precision.HIGHEST)


def body(dataset, targets, indices, particles, spread):
    n_feat = lax.axis_size("feat")
    batch_x = jnp.take(dataset, indices, axis=0)
    batch_t = jnp.take(targets, indices, axis=0)
    data_ratio = dataset.shape[0] / indices.shape[0]
    scale_h = spread[0].astype(jnp.float32)
    all_rows = lax.all_gather(particles, "dp", axis=0, tiled=True)
    count_all = all_rows.shape[0]
    rows_own = particles.shape[0]
    inner_part = contract(particles, all_rows)
    theta_all = all_rows.astype(jnp.float32)
    sq_part = jnp.sum(theta_all * theta_all, axis=1)
    packed = lax.psum(jnp.concatenate([inner_part, sq_part[None, :]], axis=0), "feat")
    inner = packed[:rows_own]
    norms_b = packed[rows_own]
    own_sq = lax.dynamic_slice_in_dim(norms_b, lax.axis_index("dp") * rows_own, rows_own, 0)
    partial_t = contract(all_rows, batch_x).astype(jnp.bfloat16)
    partial_t = partial_t.reshape(n_feat, count_all // n_feat, partial_t.shape[1])
    pieces = lax.all_to_all(partial_t, "feat", 0, 0, tiled=True)
    own_logits_t = jnp.sum(pieces.astype(jnp.float32), axis=0)
    own_residual_t = (batch_t[None, :] - jax.nn.sigmoid(own_logits_t)).astype(jnp.bfloat16)
    spread_res = jnp.broadcast_to(own_residual_t[None], (n_feat,) + own_residual_t.shape)
    residual_t = lax.all_to_all(spread_res, "feat", 0, 0, tiled=True).reshape(count_all, -1)
    grad_part = jnp.dot(residual_t, batch_x, preferred_element_type=jnp.float32)
    gradient = lax.all_gather(
        lax.psum_scatter(grad_part, "dp", scatter_dimension=0, tiled=True),
        "dp", axis=0, tiled=True,
    )
    score = data_ratio * gradient - theta_all
    kernel = jnp.exp(-(own_sq[:, None] + norms_b[None, :] - 2.0 * inner) / scale_h)
    pushed = exact_dot(kernel, score)
    pulled = exact_dot(kernel, theta_all)
    weight = jnp.sum(kernel, axis=1)
    attraction = pushed / count_all
    repulsion = (particles.astype(jnp.float32) * weight[:, None] - pulled) / count_all
    return attraction, repulsion


def solution(mesh):
    return jax.shard_map(
        body,
        mesh=mesh,
        in_specs=(P("dp", "feat"), P("dp"), P("dp"), P("dp", "feat"), P()),
        out_specs=(P("dp", "feat"), P("dp", "feat")),
        check_vma=False,
    )
```

```python
import jax
import jax.numpy as jnp
from jax import lax
from jax.sharding import PartitionSpec as P

NCH = 2


def contract(left, right):
    return lax.dot_general(
        left, right, (((1,), (1,)), ((), ())), preferred_element_type=jnp.float32
    )


def exact_dot(left, right):
    return jnp.dot(left, right, precision=lax.Precision.HIGHEST)


def step(dataset, targets, indices, particles, spread):
    n_feat = lax.axis_size("feat")
    batch_x = jnp.take(dataset, indices, axis=0)
    batch_t = jnp.take(targets, indices, axis=0)
    data_ratio = dataset.shape[0] / indices.shape[0]
    scale_h = spread[0].astype(jnp.float32)
    all_rows = lax.all_gather(particles, "dp", axis=0, tiled=True)
    count_all = all_rows.shape[0]
    rows_own = particles.shape[0]
    inner_part = contract(particles, all_rows)
    theta_all = all_rows.astype(jnp.float32)
    sq_part = jnp.sum(theta_all * theta_all, axis=1)
    packed = lax.psum(jnp.concatenate([inner_part, sq_part[None, :]], axis=0), "feat")
    inner = packed[:rows_own]
    norms_b = packed[rows_own]
    own_sq = lax.dynamic_slice_in_dim(norms_b, lax.axis_index("dp") * rows_own, rows_own, 0)
    kernel = jnp.exp(-(own_sq[:, None] + norms_b[None, :] - 2.0 * inner) / scale_h)
    chunk = count_all // NCH
    terms = []

    def issue_dp(c, grad_part):
        grad_own = lax.psum_scatter(grad_part, "dp", scatter_dimension=0, tiled=True)
        gradient = lax.all_gather(grad_own, "dp", axis=0, tiled=True)
        score = data_ratio * gradient - theta_all[c * chunk:(c + 1) * chunk]
        terms.append(exact_dot(kernel[:, c * chunk:(c + 1) * chunk], score))

    grad_part = None
    for c in range(NCH):
        rows_c = all_rows[c * chunk:(c + 1) * chunk]
        partial_t = contract(rows_c, batch_x).astype(jnp.bfloat16)
        if grad_part is not None:
            partial_t, grad_part = lax.optimization_barrier((partial_t, grad_part))
            issue_dp(c - 1, grad_part)
        partial_t = partial_t.reshape(n_feat, chunk // n_feat, partial_t.shape[1])
        pieces = lax.all_to_all(partial_t, "feat", 0, 0, tiled=True)
        own_logits_t = jnp.sum(pieces.astype(jnp.float32), axis=0)
        own_residual_t = (batch_t[None, :] - jax.nn.sigmoid(own_logits_t)).astype(jnp.bfloat16)
        spread_res = jnp.broadcast_to(own_residual_t[None], (n_feat,) + own_residual_t.shape)
        residual_t = lax.all_to_all(spread_res, "feat", 0, 0, tiled=True).reshape(chunk, -1)
        grad_part = jnp.dot(residual_t, batch_x, preferred_element_type=jnp.float32)
    issue_dp(NCH - 1, grad_part)
    pushed = terms[0]
    for term in terms[1:]:
        pushed = pushed + term
    pulled = exact_dot(kernel, theta_all)
    weight = jnp.sum(kernel, axis=1)
    attraction = pushed / count_all
    repulsion = (particles.astype(jnp.float32) * weight[:, None] - pulled) / count_all
    return attraction, repulsion


def solution(mesh):
    return jax.shard_map(
        step,
        mesh=mesh,
        in_specs=(P("dp", "feat"), P("dp"), P("dp"), P("dp", "feat"), P()),
        out_specs=(P("dp", "feat"), P("dp", "feat")),
        check_vma=False,
    )
```

```python
import jax
import jax.numpy as jnp
from jax import lax
from jax.sharding import PartitionSpec as P


def contract(left, right):
    return lax.dot_general(
        left, right, (((1,), (1,)), ((), ())), preferred_element_type=jnp.float32
    )


def exact_dot(left, right):
    return jnp.dot(left, right, precision=lax.Precision.HIGHEST)


def step(dataset, targets, indices, particles, spread):
    n_feat = lax.axis_size("feat")
    batch_x = jnp.take(dataset, indices, axis=0)
    batch_t = jnp.take(targets, indices, axis=0)
    data_ratio = dataset.shape[0] / indices.shape[0]
    scale_h = spread[0].astype(jnp.float32)
    all_rows = lax.all_gather(particles, "dp", axis=0, tiled=True)
    count_all = all_rows.shape[0]
    rows_own = particles.shape[0]
    inner_part = contract(particles, all_rows)
    theta_all = all_rows.astype(jnp.float32)
    sq_part = jnp.sum(theta_all * theta_all, axis=1)
    to_sum = jnp.concatenate([inner_part, sq_part[None, :]], axis=0)
    partial_t = contract(all_rows, batch_x).astype(jnp.bfloat16)
    partial_t = partial_t.reshape(n_feat, count_all // n_feat, partial_t.shape[1])
    pieces = lax.all_to_all(partial_t, "feat", 0, 0, tiled=True)
    to_sum, pieces = lax.optimization_barrier((to_sum, pieces))
    packed = lax.psum(to_sum, "feat")
    own_logits_t = jnp.sum(pieces.astype(jnp.float32), axis=0)
    own_residual_t = (batch_t[None, :] - jax.nn.sigmoid(own_logits_t)).astype(jnp.bfloat16)
    spread_res = jnp.broadcast_to(own_residual_t[None], (n_feat,) + own_residual_t.shape)
    residual_t = lax.all_to_all(spread_res, "feat", 0, 0, tiled=True).reshape(count_all, -1)
    inner = packed[:rows_own]
    norms_b = packed[rows_own]
    own_sq = lax.dynamic_slice_in_dim(norms_b, lax.axis_index("dp") * rows_own, rows_own, 0)
    grad_part = jnp.dot(residual_t, batch_x, preferred_element_type=jnp.float32)
    n_dp = lax.axis_size("dp")
    grad_pieces = lax.all_to_all(
        grad_part.reshape(n_dp, rows_own, grad_part.shape[1]), "dp", 0, 0, tiled=True
    )
    grad_own = jnp.sum(grad_pieces, axis=0)
    gradient = lax.all_to_all(
        jnp.broadcast_to(grad_own[None], (n_dp,) + grad_own.shape), "dp", 0, 0, tiled=True
    ).reshape(count_all, -1)
    score = data_ratio * gradient - theta_all
    kernel = jnp.exp(-(own_sq[:, None] + norms_b[None, :] - 2.0 * inner) / scale_h)
    pushed = exact_dot(kernel, score)
    pulled = exact_dot(kernel, theta_all)
    weight = jnp.sum(kernel, axis=1)
    attraction = pushed / count_all
    repulsion = (particles.astype(jnp.float32) * weight[:, None] - pulled) / count_all
    return attraction, repulsion


def solution(mesh):
    return jax.shard_map(
        step,
        mesh=mesh,
        in_specs=(P("dp", "feat"), P("dp"), P("dp"), P("dp", "feat"), P()),
        out_specs=(P("dp", "feat"), P("dp", "feat")),
        check_vma=False,
    )
```

```python
import jax
import jax.numpy as jnp
from jax import lax
from jax.sharding import Mesh, PartitionSpec as P


DP = ("y", "xl", "c")
YX = ("y", "xl")
FT = ("xh", "z")


def contract(left, right):
    return lax.dot_general(
        left, right, (((1,), (1,)), ((), ())), preferred_element_type=jnp.float32
    )


def exact_dot(left, right):
    return jnp.dot(left, right, precision=lax.Precision.HIGHEST)


def step(dataset, targets, indices, particles, spread):
    n_feat = lax.axis_size(FT)
    batch_x = jnp.take(dataset, indices, axis=0)
    batch_t = jnp.take(targets, indices, axis=0)
    data_ratio = dataset.shape[0] / indices.shape[0]
    scale_h = spread[0].astype(jnp.float32)
    all_rows = lax.all_gather(particles, DP, axis=0, tiled=True)
    count_all = all_rows.shape[0]
    rows_own = particles.shape[0]
    inner_part = contract(particles, all_rows)
    theta_all = all_rows.astype(jnp.float32)
    sq_part = jnp.sum(theta_all * theta_all, axis=1)
    to_sum = jnp.concatenate([inner_part, sq_part[None, :]], axis=0)
    partial_t = contract(all_rows, batch_x).astype(jnp.bfloat16)
    partial_t = partial_t.reshape(n_feat, count_all // n_feat, partial_t.shape[1])
    pieces = lax.all_to_all(partial_t, FT, 0, 0, tiled=True)
    own_logits_t = jnp.sum(pieces.astype(jnp.float32), axis=0)
    own_residual_t = (batch_t[None, :] - jax.nn.sigmoid(own_logits_t)).astype(jnp.bfloat16)
    spread_res = jnp.broadcast_to(own_residual_t[None], (n_feat,) + own_residual_t.shape)
    residual_t = lax.all_to_all(spread_res, FT, 0, 0, tiled=True).reshape(count_all, -1)
    packed = lax.psum(to_sum, FT)
    inner = packed[:rows_own]
    norms_b = packed[rows_own]
    own_sq = lax.dynamic_slice_in_dim(norms_b, lax.axis_index(DP) * rows_own, rows_own, 0)
    grad_part = jnp.dot(residual_t, batch_x, preferred_element_type=jnp.float32)
    n_c = lax.axis_size("c")
    n_yx = lax.axis_size(YX)
    width = grad_part.shape[1]
    pair = lax.all_to_all(
        grad_part.reshape(n_yx, n_c, rows_own, width), "c", 1, 1, tiled=True
    )
    pair_sum = jnp.sum(pair, axis=1)
    grad_own = jnp.sum(lax.all_to_all(pair_sum, YX, 0, 0, tiled=True), axis=0)
    chips = lax.all_to_all(
        jnp.broadcast_to(grad_own[None], (n_yx,) + grad_own.shape), YX, 0, 0, tiled=True
    )
    gradient = lax.all_to_all(
        jnp.broadcast_to(chips[:, None], (n_yx, n_c, rows_own, width)), "c", 1, 1, tiled=True
    ).reshape(count_all, width)
    score = data_ratio * gradient - theta_all
    kernel = jnp.exp(-(own_sq[:, None] + norms_b[None, :] - 2.0 * inner) / scale_h)
    pushed = exact_dot(kernel, score)
    pulled = exact_dot(kernel, theta_all)
    weight = jnp.sum(kernel, axis=1)
    attraction = pushed / count_all
    repulsion = (particles.astype(jnp.float32) * weight[:, None] - pulled) / count_all
    return attraction, repulsion


def solution(mesh):
    fine = Mesh(mesh.devices.reshape(4, 2, 2, 2, 4), DP + FT)
    return jax.shard_map(
        step,
        mesh=fine,
        in_specs=(P(DP, FT), P(DP), P(DP), P(DP, FT), P()),
        out_specs=(P(DP, FT), P(DP, FT)),
        check_vma=False,
    )
```

```python
import jax
import jax.numpy as jnp
from jax import lax
from jax.sharding import Mesh, PartitionSpec as P


DP = ("y", "xl", "c")
YX = ("y", "xl")
FT = ("xh", "z")


def contract(left, right):
    return lax.dot_general(
        left, right, (((1,), (1,)), ((), ())), preferred_element_type=jnp.float32
    )


def exact_dot(left, right):
    return jnp.dot(left, right, precision=lax.Precision.HIGHEST)


def step(dataset, targets, indices, particles, spread):
    n_feat = lax.axis_size(FT)
    batch_x = jnp.take(dataset, indices, axis=0)
    data_ratio = dataset.shape[0] / indices.shape[0]
    scale_h = spread[0].astype(jnp.float32)
    n_c = lax.axis_size("c")
    n_yx = lax.axis_size(YX)
    pair_rows = lax.all_to_all(
        jnp.broadcast_to(particles[None], (n_c,) + particles.shape), "c", 0, 0, tiled=True
    )
    all_rows = lax.all_to_all(
        jnp.broadcast_to(pair_rows[None], (n_yx,) + pair_rows.shape), YX, 0, 0, tiled=True
    ).reshape(-1, particles.shape[1])
    count_all = all_rows.shape[0]
    rows_own = particles.shape[0]
    inner_part = contract(particles, all_rows)
    theta_all = all_rows.astype(jnp.float32)
    sq_part = jnp.sum(theta_all * theta_all, axis=1)
    to_sum = jnp.concatenate([inner_part, sq_part[None, :]], axis=0)
    partial_t = contract(all_rows, batch_x).astype(jnp.bfloat16)
    partial_t = partial_t.reshape(n_feat, count_all // n_feat, partial_t.shape[1])
    late = lax.optimization_barrier((targets, indices, partial_t))
    partial_t = late[2]
    batch_t = jnp.take(late[0], late[1], axis=0)
    pieces = lax.all_to_all(partial_t, FT, 0, 0, tiled=True)
    own_logits_t = jnp.sum(pieces.astype(jnp.float32), axis=0)
    own_residual_t = (batch_t[None, :] - jax.nn.sigmoid(own_logits_t)).astype(jnp.bfloat16)
    spread_res = jnp.broadcast_to(own_residual_t[None], (n_feat,) + own_residual_t.shape)
    residual_t = lax.all_to_all(spread_res, FT, 0, 0, tiled=True).reshape(count_all, -1)
    packed = lax.psum(to_sum, FT)
    inner = packed[:rows_own]
    norms_b = packed[rows_own]
    own_sq = lax.dynamic_slice_in_dim(norms_b, lax.axis_index(DP) * rows_own, rows_own, 0)
    grad_part = jnp.dot(residual_t, batch_x, preferred_element_type=jnp.float32)
    width = grad_part.shape[1]
    pair = lax.all_to_all(
        grad_part.reshape(n_yx, n_c, rows_own, width), "c", 1, 1, tiled=True
    )
    pair_sum = jnp.sum(pair, axis=1)
    grad_own = jnp.sum(lax.all_to_all(pair_sum, YX, 0, 0, tiled=True), axis=0)
    chips = lax.all_to_all(
        jnp.broadcast_to(grad_own[None], (n_yx,) + grad_own.shape), YX, 0, 0, tiled=True
    )
    gradient = lax.all_to_all(
        jnp.broadcast_to(chips[:, None], (n_yx, n_c, rows_own, width)), "c", 1, 1, tiled=True
    ).reshape(count_all, width)
    score = data_ratio * gradient - theta_all
    kernel = jnp.exp(-(own_sq[:, None] + norms_b[None, :] - 2.0 * inner) / scale_h)
    pushed = exact_dot(kernel, score)
    pulled = exact_dot(kernel, theta_all)
    weight = jnp.sum(kernel, axis=1)
    attraction = pushed / count_all
    repulsion = (particles.astype(jnp.float32) * weight[:, None] - pulled) / count_all
    return attraction, repulsion


def solution(mesh):
    fine = Mesh(mesh.devices.reshape(4, 2, 2, 2, 4), DP + FT)
    return jax.shard_map(
        step,
        mesh=fine,
        in_specs=(P(DP, FT), P(DP), P(DP), P(DP, FT), P()),
        out_specs=(P(DP, FT), P(DP, FT)),
        check_vma=False,
    )
```

```python
import jax
import jax.numpy as jnp
from jax import lax
from jax.sharding import Mesh, PartitionSpec as P


DP = ("y", "xl", "c")
YX = ("y", "xl")
FT = ("xh", "z")


def contract(left, right):
    return lax.dot_general(
        left, right, (((1,), (1,)), ((), ())), preferred_element_type=jnp.float32
    )


def exact_dot(left, right):
    return jnp.dot(left, right, precision=lax.Precision.HIGHEST)


def step(dataset, targets, indices, particles, spread):
    n_feat = lax.axis_size(FT)
    batch_x = jnp.take(dataset, indices, axis=0)
    data_ratio = dataset.shape[0] / indices.shape[0]
    scale_h = spread[0].astype(jnp.float32)
    n_c = lax.axis_size("c")
    n_yx = lax.axis_size(YX)
    pair_rows = lax.all_to_all(
        jnp.broadcast_to(particles[None], (n_c,) + particles.shape), "c", 0, 0, tiled=True
    )
    all_rows = lax.all_to_all(
        jnp.broadcast_to(pair_rows[None], (n_yx,) + pair_rows.shape), YX, 0, 0, tiled=True
    ).reshape(-1, particles.shape[1])
    count_all = all_rows.shape[0]
    rows_own = particles.shape[0]
    inner_part = contract(particles, all_rows)
    theta_all = all_rows.astype(jnp.float32)
    sq_part = jnp.sum(theta_all * theta_all, axis=1)
    to_sum = jnp.concatenate([inner_part, sq_part[None, :]], axis=0)
    per_peer = -(-to_sum.shape[0] // n_feat)
    to_sum = jnp.pad(to_sum, ((0, per_peer * n_feat - to_sum.shape[0]), (0, 0)))
    me = lax.axis_index(FT)
    inner_own = lax.dynamic_slice_in_dim(to_sum, me * per_peer, per_peer, 0)
    for k in range(1, n_feat):
        piece = lax.dynamic_slice_in_dim(to_sum, ((me + k) % n_feat) * per_peer, per_peer, 0)
        inner_own = inner_own + lax.ppermute(
            piece, FT, [(i, (i + k) % n_feat) for i in range(n_feat)]
        )
    partial_t = contract(all_rows, batch_x).astype(jnp.bfloat16)
    partial_t = partial_t.reshape(n_feat, count_all // n_feat, partial_t.shape[1])
    late = lax.optimization_barrier((targets, indices, partial_t))
    partial_t = late[2]
    batch_t = jnp.take(late[0], late[1], axis=0)
    pieces = lax.all_to_all(partial_t, FT, 0, 0, tiled=True)
    own_logits_t = jnp.sum(pieces.astype(jnp.float32), axis=0)
    own_residual_t = (batch_t[None, :] - jax.nn.sigmoid(own_logits_t)).astype(jnp.bfloat16)
    spread_res = jnp.broadcast_to(own_residual_t[None], (n_feat,) + own_residual_t.shape)
    residual_t = lax.all_to_all(spread_res, FT, 0, 0, tiled=True).reshape(count_all, -1)
    got = [inner_own] + [
        lax.ppermute(inner_own, FT, [(i, (i + k) % n_feat) for i in range(n_feat)])
        for k in range(1, n_feat)
    ]
    order = (me - jnp.arange(n_feat)) % n_feat
    packed = jnp.take(jnp.stack(got), order, axis=0).reshape(-1, count_all)
    inner = packed[:rows_own]
    norms_b = packed[rows_own]
    own_sq = lax.dynamic_slice_in_dim(norms_b, lax.axis_index(DP) * rows_own, rows_own, 0)
    grad_part = jnp.dot(residual_t, batch_x, preferred_element_type=jnp.float32)
    width = grad_part.shape[1]
    pair = lax.all_to_all(
        grad_part.reshape(n_yx, n_c, rows_own, width), "c", 1, 1, tiled=True
    )
    pair_sum = jnp.sum(pair, axis=1)
    grad_own = jnp.sum(lax.all_to_all(pair_sum, YX, 0, 0, tiled=True), axis=0)
    chips = lax.all_to_all(
        jnp.broadcast_to(grad_own[None], (n_yx,) + grad_own.shape), YX, 0, 0, tiled=True
    )
    gradient = lax.all_to_all(
        jnp.broadcast_to(chips[:, None], (n_yx, n_c, rows_own, width)), "c", 1, 1, tiled=True
    ).reshape(count_all, width)
    score = data_ratio * gradient - theta_all
    kernel = jnp.exp(-(own_sq[:, None] + norms_b[None, :] - 2.0 * inner) / scale_h)
    pushed = exact_dot(kernel, score)
    pulled = exact_dot(kernel, theta_all)
    weight = jnp.sum(kernel, axis=1)
    attraction = pushed / count_all
    repulsion = (particles.astype(jnp.float32) * weight[:, None] - pulled) / count_all
    return attraction, repulsion


def solution(mesh):
    fine = Mesh(mesh.devices.reshape(4, 2, 2, 2, 4), DP + FT)
    return jax.shard_map(
        step,
        mesh=fine,
        in_specs=(P(DP, FT), P(DP), P(DP), P(DP, FT), P()),
        out_specs=(P(DP, FT), P(DP, FT)),
        check_vma=False,
    )
```

```python
import jax
import jax.numpy as jnp
from jax import lax
from jax.sharding import Mesh, PartitionSpec as P


DP = ("y", "xl", "c")
YX = ("y", "xl")
FT = ("xh", "z")


def contract(left, right):
    return lax.dot_general(
        left, right, (((1,), (1,)), ((), ())), preferred_element_type=jnp.float32
    )


def exact_dot(left, right):
    return jnp.dot(left, right, precision=lax.Precision.HIGHEST)


def step(dataset, targets, indices, particles, spread):
    n_feat = lax.axis_size(FT)
    batch_x = jnp.take(dataset, indices, axis=0)
    data_ratio = dataset.shape[0] / indices.shape[0]
    scale_h = spread[0].astype(jnp.float32)
    n_c = lax.axis_size("c")
    n_yx = lax.axis_size(YX)
    n_dp = lax.axis_size(DP)
    all_rows = lax.all_to_all(
        jnp.broadcast_to(particles[None], (n_dp,) + particles.shape), DP, 0, 0, tiled=True
    ).reshape(-1, particles.shape[1])
    count_all = all_rows.shape[0]
    rows_own = particles.shape[0]
    inner_part = contract(particles, all_rows)
    theta_all = all_rows.astype(jnp.float32)
    sq_part = jnp.sum(theta_all * theta_all, axis=1)
    to_sum = jnp.concatenate([inner_part, sq_part[None, :]], axis=0)
    partial_t = contract(all_rows, batch_x).astype(jnp.bfloat16)
    partial_t = partial_t.reshape(n_feat, count_all // n_feat, partial_t.shape[1])
    late = lax.optimization_barrier((targets, indices, partial_t))
    partial_t = late[2]
    batch_t = jnp.take(late[0], late[1], axis=0)
    pieces = lax.all_to_all(partial_t, FT, 0, 0, tiled=True)
    own_logits_t = jnp.sum(pieces.astype(jnp.float32), axis=0)
    own_residual_t = (batch_t[None, :] - jax.nn.sigmoid(own_logits_t)).astype(jnp.bfloat16)
    spread_res = jnp.broadcast_to(own_residual_t[None], (n_feat,) + own_residual_t.shape)
    residual_t = lax.all_to_all(spread_res, FT, 0, 0, tiled=True).reshape(count_all, -1)
    packed = lax.psum(to_sum, FT)
    inner = packed[:rows_own]
    norms_b = packed[rows_own]
    own_sq = lax.dynamic_slice_in_dim(norms_b, lax.axis_index(DP) * rows_own, rows_own, 0)
    grad_part = jnp.dot(residual_t, batch_x, preferred_element_type=jnp.float32)
    width = grad_part.shape[1]
    pair = lax.all_to_all(
        grad_part.reshape(n_yx, n_c, rows_own, width), "c", 1, 1, tiled=True
    )
    pair_sum = jnp.sum(pair, axis=1)
    grad_own = jnp.sum(lax.all_to_all(pair_sum, YX, 0, 0, tiled=True), axis=0)
    chips = lax.all_to_all(
        jnp.broadcast_to(grad_own[None], (n_yx,) + grad_own.shape), YX, 0, 0, tiled=True
    )
    gradient = lax.all_to_all(
        jnp.broadcast_to(chips[:, None], (n_yx, n_c, rows_own, width)), "c", 1, 1, tiled=True
    ).reshape(count_all, width)
    score = data_ratio * gradient - theta_all
    kernel = jnp.exp(-(own_sq[:, None] + norms_b[None, :] - 2.0 * inner) / scale_h)
    pushed = exact_dot(kernel, score)
    pulled = exact_dot(kernel, theta_all)
    weight = jnp.sum(kernel, axis=1)
    attraction = pushed / count_all
    repulsion = (particles.astype(jnp.float32) * weight[:, None] - pulled) / count_all
    return attraction, repulsion


def solution(mesh):
    fine = Mesh(mesh.devices.reshape(4, 2, 2, 2, 4), DP + FT)
    return jax.shard_map(
        step,
        mesh=fine,
        in_specs=(P(DP, FT), P(DP), P(DP), P(DP, FT), P()),
        out_specs=(P(DP, FT), P(DP, FT)),
        check_vma=False,
    )
```

```python
import jax
import jax.numpy as jnp
from jax import lax
from jax.sharding import Mesh, PartitionSpec as P


DP = ("y", "xl", "c")
YX = ("y", "xl")
FT = ("xh", "z")


def contract(left, right):
    return lax.dot_general(
        left, right, (((1,), (1,)), ((), ())), preferred_element_type=jnp.float32
    )


def exact_dot(left, right):
    return jnp.dot(left, right, precision=lax.Precision.HIGHEST)


def step(dataset, targets, indices, particles, spread):
    n_feat = lax.axis_size(FT)
    batch_x = jnp.take(dataset, indices, axis=0)
    data_ratio = dataset.shape[0] / indices.shape[0]
    scale_h = spread[0].astype(jnp.float32)
    n_c = lax.axis_size("c")
    n_yx = lax.axis_size(YX)
    n_dp = lax.axis_size(DP)
    all_rows = lax.all_to_all(
        jnp.broadcast_to(particles[None], (n_dp,) + particles.shape), DP, 0, 0, tiled=True
    ).reshape(-1, particles.shape[1])
    count_all = all_rows.shape[0]
    rows_own = particles.shape[0]
    inner_part = contract(particles, all_rows)
    theta_all = all_rows.astype(jnp.float32)
    sq_part = jnp.sum(theta_all * theta_all, axis=1)
    to_sum = jnp.concatenate([inner_part, sq_part[None, :]], axis=0)
    partial_t = contract(all_rows, batch_x).astype(jnp.bfloat16)
    partial_t = partial_t.reshape(n_feat, count_all // n_feat, partial_t.shape[1])
    late = lax.optimization_barrier((targets, indices, partial_t))
    partial_t = late[2]
    batch_t = jnp.take(late[0], late[1], axis=0)
    pieces = lax.all_to_all(partial_t, FT, 0, 0, tiled=True)
    own_logits_t = jnp.sum(pieces.astype(jnp.float32), axis=0)
    own_residual_t = (batch_t[None, :] - jax.nn.sigmoid(own_logits_t)).astype(jnp.bfloat16)
    spread_res = jnp.broadcast_to(own_residual_t[None], (n_feat,) + own_residual_t.shape)
    residual_t = lax.all_to_all(spread_res, FT, 0, 0, tiled=True).reshape(count_all, -1)
    packed = lax.psum(to_sum, FT)
    inner = packed[:rows_own]
    norms_b = packed[rows_own]
    own_sq = lax.dynamic_slice_in_dim(norms_b, lax.axis_index(DP) * rows_own, rows_own, 0)
    grad_part = jnp.dot(residual_t, batch_x, preferred_element_type=jnp.float32)
    width = grad_part.shape[1]
    pair = lax.all_to_all(
        grad_part.reshape(n_yx, n_c, rows_own, width), "c", 1, 1, tiled=True
    )
    pair_sum = jnp.sum(pair, axis=1)
    grad_own = jnp.sum(lax.all_to_all(pair_sum, YX, 0, 0, tiled=True), axis=0)
    chips = lax.all_to_all(
        jnp.broadcast_to(grad_own[None], (n_yx,) + grad_own.shape), YX, 0, 0, tiled=True
    )
    kernel = jnp.exp(-(own_sq[:, None] + norms_b[None, :] - 2.0 * inner) / scale_h)
    kernel4 = kernel.reshape(rows_own, n_yx, n_c, rows_own)
    theta4 = theta_all.reshape(n_yx, n_c, rows_own, width)
    me_c = lax.axis_index("c")
    mine = lambda a, axis: lax.dynamic_index_in_dim(a, me_c, axis, keepdims=False)
    score_own = data_ratio * chips - mine(theta4, 1)
    pushed = lax.optimization_barrier(exact_dot(
        mine(kernel4, 2).reshape(rows_own, -1), score_own.reshape(-1, width)
    ))
    both = lax.all_to_all(
        jnp.broadcast_to(chips[:, None], (n_yx, n_c, rows_own, width)), "c", 1, 1, tiled=True
    )
    other = 1 - me_c
    theirs = lambda a, axis: lax.dynamic_index_in_dim(a, other, axis, keepdims=False)
    score_other = data_ratio * theirs(both, 1) - theirs(theta4, 1)
    pushed = pushed + exact_dot(
        theirs(kernel4, 2).reshape(rows_own, -1), score_other.reshape(-1, width)
    )
    pulled = exact_dot(kernel, theta_all)
    weight = jnp.sum(kernel, axis=1)
    attraction = pushed / count_all
    repulsion = (particles.astype(jnp.float32) * weight[:, None] - pulled) / count_all
    return attraction, repulsion


def solution(mesh):
    fine = Mesh(mesh.devices.reshape(4, 2, 2, 2, 4), DP + FT)
    return jax.shard_map(
        step,
        mesh=fine,
        in_specs=(P(DP, FT), P(DP), P(DP), P(DP, FT), P()),
        out_specs=(P(DP, FT), P(DP, FT)),
        check_vma=False,
    )
```

```python
import jax
import jax.numpy as jnp
from jax import lax
from jax.sharding import Mesh, PartitionSpec as P


DP = ("y", "xl", "c")
YX = ("y", "xl")
FT = ("xh", "z")


def contract(left, right):
    return lax.dot_general(
        left, right, (((1,), (1,)), ((), ())), preferred_element_type=jnp.float32
    )


def exact_dot(left, right):
    return jnp.dot(left, right, precision=lax.Precision.HIGHEST)


def step(dataset, targets, indices, particles, spread):
    n_feat = lax.axis_size(FT)
    batch_x = jnp.take(dataset, indices, axis=0)
    data_ratio = dataset.shape[0] / indices.shape[0]
    scale_h = spread[0].astype(jnp.float32)
    n_c = lax.axis_size("c")
    n_yx = lax.axis_size(YX)
    n_dp = lax.axis_size(DP)
    all_rows = lax.all_to_all(
        jnp.broadcast_to(particles[None], (n_dp,) + particles.shape), DP, 0, 0, tiled=True
    ).reshape(-1, particles.shape[1])
    count_all = all_rows.shape[0]
    rows_own = particles.shape[0]
    inner_part = contract(particles, all_rows)
    theta_all = all_rows.astype(jnp.float32)
    sq_part = jnp.sum(theta_all * theta_all, axis=1)
    to_sum = jnp.concatenate([inner_part, sq_part[None, :]], axis=0)
    partial_t = contract(all_rows, batch_x).astype(jnp.bfloat16)
    partial_t = partial_t.reshape(n_feat, count_all // n_feat, partial_t.shape[1])
    late = lax.optimization_barrier((targets, indices, partial_t))
    partial_t = late[2]
    batch_t = jnp.take(late[0], late[1], axis=0)
    pieces = lax.all_to_all(partial_t, FT, 0, 0, tiled=True)
    own_logits_t = jnp.sum(pieces.astype(jnp.float32), axis=0)
    own_residual_t = (batch_t[None, :] - jax.nn.sigmoid(own_logits_t)).astype(jnp.bfloat16)
    spread_res = jnp.broadcast_to(own_residual_t[None], (n_feat,) + own_residual_t.shape)
    residual_t = lax.all_to_all(spread_res, FT, 0, 0, tiled=True).reshape(count_all, -1)
    packed = lax.psum(to_sum, FT)
    inner = packed[:rows_own]
    norms_b = packed[rows_own]
    own_sq = lax.dynamic_slice_in_dim(norms_b, lax.axis_index(DP) * rows_own, rows_own, 0)
    grad_part = jnp.dot(residual_t, batch_x, preferred_element_type=jnp.float32)
    width = grad_part.shape[1]
    me_c = lax.axis_index("c")
    swap = [(0, 1), (1, 0)]
    grad4 = grad_part.reshape(n_yx, n_c, rows_own, width)
    from_pair = lax.ppermute(
        lax.dynamic_index_in_dim(grad4, 1 - me_c, 1, keepdims=False), "c", swap
    )
    pair_sum = lax.dynamic_index_in_dim(grad4, me_c, 1, keepdims=False) + from_pair
    grad_own = jnp.sum(lax.all_to_all(pair_sum, YX, 0, 0, tiled=True), axis=0)
    chips = lax.all_to_all(
        jnp.broadcast_to(grad_own[None], (n_yx,) + grad_own.shape), YX, 0, 0, tiled=True
    )
    other_chips = lax.ppermute(chips, "c", swap)
    first = me_c == 0
    gradient = jnp.stack(
        [jnp.where(first, chips, other_chips), jnp.where(first, other_chips, chips)], axis=1
    ).reshape(count_all, width)
    score = data_ratio * gradient - theta_all
    kernel = jnp.exp(-(own_sq[:, None] + norms_b[None, :] - 2.0 * inner) / scale_h)
    pulled = exact_dot(kernel, theta_all)
    weight = jnp.sum(kernel, axis=1)
    repulsion = (particles.astype(jnp.float32) * weight[:, None] - pulled) / count_all
    pushed = exact_dot(kernel, score)
    attraction = pushed / count_all
    return attraction, repulsion


def solution(mesh):
    fine = Mesh(mesh.devices.reshape(4, 2, 2, 2, 4), DP + FT)
    return jax.shard_map(
        step,
        mesh=fine,
        in_specs=(P(DP, FT), P(DP), P(DP), P(DP, FT), P()),
        out_specs=(P(DP, FT), P(DP, FT)),
        check_vma=False,
    )
```

```python
import jax
import jax.numpy as jnp
from jax import lax
from jax.sharding import Mesh, PartitionSpec as P


DP = ("y", "xl", "c")
YX = ("y", "xl")
FT = ("xh", "z")


def contract(left, right):
    return lax.dot_general(
        left, right, (((1,), (1,)), ((), ())), preferred_element_type=jnp.float32
    )


def exact_dot(left, right):
    return jnp.dot(left, right, precision=lax.Precision.HIGHEST)


def step(dataset, targets, indices, particles, spread):
    n_feat = lax.axis_size(FT)
    batch_x = jnp.take(dataset, indices, axis=0)
    data_ratio = dataset.shape[0] / indices.shape[0]
    scale_h = spread[0].astype(jnp.float32)
    n_c = lax.axis_size("c")
    n_yx = lax.axis_size(YX)
    n_dp = lax.axis_size(DP)
    all_rows = lax.all_to_all(
        jnp.broadcast_to(particles[None], (n_dp,) + particles.shape), DP, 0, 0, tiled=True
    ).reshape(-1, particles.shape[1])
    count_all = all_rows.shape[0]
    rows_own = particles.shape[0]
    inner_part = contract(particles, all_rows)
    theta_all = all_rows.astype(jnp.float32)
    sq_part = jnp.sum(theta_all * theta_all, axis=1)
    to_sum = jnp.concatenate([inner_part, sq_part[None, :]], axis=0)
    partial_t = contract(all_rows, batch_x).astype(jnp.bfloat16)
    partial_t = partial_t.reshape(n_feat, count_all // n_feat, partial_t.shape[1])
    late = lax.optimization_barrier((targets, indices, partial_t))
    partial_t = late[2]
    batch_t = jnp.take(late[0], late[1], axis=0)
    pieces = lax.all_to_all(partial_t, FT, 0, 0, tiled=True)
    own_logits_t = jnp.sum(pieces.astype(jnp.float32), axis=0)
    own_residual_t = (batch_t[None, :] - jax.nn.sigmoid(own_logits_t)).astype(jnp.bfloat16)
    spread_res = jnp.broadcast_to(own_residual_t[None], (n_feat,) + own_residual_t.shape)
    residual_t = lax.all_to_all(spread_res, FT, 0, 0, tiled=True).reshape(count_all, -1)
    packed = lax.psum(to_sum, FT)
    inner = packed[:rows_own]
    norms_b = packed[rows_own]
    own_sq = lax.dynamic_slice_in_dim(norms_b, lax.axis_index(DP) * rows_own, rows_own, 0)
    me_c = lax.axis_index("c")
    swap = [(0, 1), (1, 0)]
    width = batch_x.shape[1]
    res4 = residual_t.reshape(n_yx, n_c, rows_own, -1)

    def grad_half(c):
        rows = lax.dynamic_index_in_dim(res4, c, 1, keepdims=False).reshape(n_yx * rows_own, -1)
        grad = jnp.dot(rows, batch_x, preferred_element_type=jnp.float32)
        return grad.reshape(n_yx, rows_own, width)

    from_pair = lax.ppermute(grad_half(1 - me_c), "c", swap)
    own_half = lax.optimization_barrier(grad_half(me_c))
    pair_sum = own_half + from_pair
    grad_own = jnp.sum(lax.all_to_all(pair_sum, YX, 0, 0, tiled=True), axis=0)
    chips = lax.all_to_all(
        jnp.broadcast_to(grad_own[None], (n_yx,) + grad_own.shape), YX, 0, 0, tiled=True
    )
    other_chips = lax.ppermute(chips, "c", swap)
    first = me_c == 0
    gradient = jnp.stack(
        [jnp.where(first, chips, other_chips), jnp.where(first, other_chips, chips)], axis=1
    ).reshape(count_all, width)
    score = data_ratio * gradient - theta_all
    kernel = jnp.exp(-(own_sq[:, None] + norms_b[None, :] - 2.0 * inner) / scale_h)
    pulled = exact_dot(kernel, theta_all)
    weight = jnp.sum(kernel, axis=1)
    repulsion = (particles.astype(jnp.float32) * weight[:, None] - pulled) / count_all
    pushed = exact_dot(kernel, score)
    attraction = pushed / count_all
    return attraction, repulsion


def solution(mesh):
    fine = Mesh(mesh.devices.reshape(4, 2, 2, 2, 4), DP + FT)
    return jax.shard_map(
        step,
        mesh=fine,
        in_specs=(P(DP, FT), P(DP), P(DP), P(DP, FT), P()),
        out_specs=(P(DP, FT), P(DP, FT)),
        check_vma=False,
    )
```
